256 devices in a mesh: snap: 4 (over x), line: 64 (over z, y, core).
Axes of the slice: x: 4, y: 4, z: 8, core: 2. Of those that a mesh axis runs over, the one named last changes fastest.
Arguments:
- ptdf_rows: float32 [8192, 20480], P('line'), may hold values from -4 to 4
- plan: float32 [5120, 2048], P(('snap', 'line')), may hold values from 0 to 0.15
- unit_bus: int32 [5120], replicated, may hold values from 0 to 20479
- min_up: int32 [5120], P(('snap', 'line')), may hold values from 1 to 24, as said below
- ramp_lag: int32 [5120], P(('snap', 'line')), may hold values from 1 to 6, as said below
- load_share: float32 [20480], replicated, may hold values from 0.004 to 0.04
- system_load: float32 [2048], P('snap'), may hold values from 0.6 to 1.4
- corridor_order: int32 [4], replicated, may hold values from 0 to 3, each once
- corridor_buses: int32 [4, 2], replicated, may hold values from 0 to 20479, as said below
- corridor_owner: int32 [4], replicated, may hold values from 0 to 63
- corridor_row: int32 [4], replicated, may hold values from 0 to 127
- corridor_ratio: float32 [4], replicated, may hold values from 0.5 to 2
Outputs:
- flows: float32 [8192, 2048], P('line', 'snap')
- corridor_sens: float32 [4, 20480], replicated
The draws below stay inside these ranges and needn't reach their ends.
Inputs may be any that keep to these rules, and one draw needn't show every extreme that they name: `min_up`: some unit has a window of exactly 24. `ramp_lag`: some unit has a lag of exactly 6. `corridor_buses`: the two buses of a corridor differ.
All inputs are finite; a program needn't handle non-finite values.
Results may differ from the reference program's by a relative error of at most 0.000098.
Values sent between devices are 32-bit elements; how exact they have to be, the bound alone decides.
No kernel may reach another device: no remote copies, remote signals or barrier semaphores. Data moves between devices by JAX's collectives and lax.ppermute only.
A program may use at most 128 MiB of HBM per device.

```python
import math
import jax
import jax.numpy as jnp
from jax import lax

B = 20480
G = 5120
L_DEV = 128
WMAX = 24
RAMP_MOST = 6
NC = 4
LINES = 8192
SNAPS = 2048
N_LINE = 64


def window_draw(key, most):
    first_key, second_key = jax.random.split(key)
    values = jax.random.randint(first_key, (G,), 1, most + 1).astype(jnp.int32)
    spot = jax.random.randint(second_key, (), 0, G)
    return values.at[spot].set(most).astype(jnp.int32)


def draw_min_up(key, part):
    return window_draw(jax.random.fold_in(key, 11), WMAX)


def draw_ramp_lag(key, part):
    return window_draw(jax.random.fold_in(key, 23), RAMP_MOST)


def draw_corridor_buses(key, part):
    first_key, second_key, third_key = jax.random.split(jax.random.fold_in(key, 37), 3)
    bus_from = jax.random.randint(first_key, (NC,), 0, B).astype(jnp.int32)
    bus_gap = jax.random.randint(second_key, (NC,), 1, B).astype(jnp.int32)
    bus_to = (bus_from + bus_gap) % B
    spot = jax.random.randint(third_key, (), 0, NC)
    bus_from = bus_from.at[spot].set(0)
    bus_to = bus_to.at[spot].set(B - 1)
    return jnp.stack([bus_from, bus_to], axis=1).astype(jnp.int32)


def touch_ends(drawn, stream_key, smallest, top_value):
    longest = drawn.shape.index(max(drawn.shape))
    spots = []
    for shift in (0, 1):
        where = [jax.random.randint(jax.random.fold_in(stream_key, axis), (), 0, length) for axis, length in enumerate(drawn.shape)]
        where[longest] = (where[longest] + shift) % drawn.shape[longest]
        spots.append(tuple(where))
    return drawn.at[spots[0]].set(smallest).at[spots[1]].set(top_value)


def steps_of(rng, dims, cuts, low, top_value):
    factor_of = 1.0
    for axis_at, shards_of in cuts:
        heights = jax.random.uniform(jax.random.fold_in(jax.random.fold_in(rng, 6), axis_at), (shards_of,), jnp.float32, low / len(cuts), top_value / len(cuts))
        factor_of = factor_of * jnp.repeat(jnp.exp(heights), dims[axis_at] // shards_of).reshape((-1,) + (1,) * (len(dims) - 1 - axis_at))
    return factor_of


def centred(rng, dims, spread, limit, cuts=(), kind=jnp.bfloat16):
    gain = steps_of(rng, dims, cuts, -0.22, 0.18) if cuts else 1.0
    drawn = jax.random.normal(rng, dims, jnp.float32) * spread * gain
    return jnp.minimum(jnp.maximum(drawn, -limit), limit).astype(kind)


def setup_inputs(seed: int = 0) -> dict:
    arg_keys = jax.random.split(jax.random.key(seed), 13)
    return {
        "ptdf_rows": centred(arg_keys[0], (LINES, B), 0.25, 4.0, ((0, 64),), jnp.float32),
        "plan": jnp.clip(0.15 * jax.random.uniform(arg_keys[1], (G, SNAPS), jnp.float32) ** steps_of(arg_keys[1], (G, SNAPS), ((0, 256),), -0.2, 0.2), 0.0, 0.15),
        "unit_bus": touch_ends(jax.random.randint(arg_keys[2], (G,), 0, B), jax.random.fold_in(arg_keys[2], 1), 0, B - 1).astype(jnp.int32),
        "min_up": draw_min_up(jax.random.fold_in(arg_keys[12], 71), 0),
        "ramp_lag": draw_ramp_lag(jax.random.fold_in(arg_keys[12], 71), 0),
        "load_share": jnp.clip(jnp.exp(jax.random.uniform(arg_keys[5], (B,), jnp.float32, math.log(0.004), math.log(0.04))), 0.004, 0.04),
        "system_load": jnp.clip(0.6 + 0.79999995 * jax.random.uniform(arg_keys[6], (SNAPS,), jnp.float32) ** steps_of(arg_keys[6], (SNAPS,), ((0, 4),), -0.2, 0.2), 0.6, 1.4),
        "corridor_order": jax.random.permutation(arg_keys[7], NC).astype(jnp.int32),
        "corridor_buses": draw_corridor_buses(jax.random.fold_in(arg_keys[12], 71), 0),
        "corridor_owner": touch_ends(jax.random.randint(arg_keys[9], (NC,), 0, N_LINE), jax.random.fold_in(arg_keys[9], 1), 0, N_LINE - 1).astype(jnp.int32),
        "corridor_row": touch_ends(jax.random.randint(arg_keys[10], (NC,), 0, L_DEV), jax.random.fold_in(arg_keys[10], 1), 0, L_DEV - 1).astype(jnp.int32),
        "corridor_ratio": jnp.clip(jnp.exp(jax.random.uniform(arg_keys[11], (NC,), jnp.float32, math.log(0.5), math.log(2.0))), 0.5, 2.0),
    }


ramp_gain = 0.5


def reference(ptdf_rows, plan, unit_bus, min_up, ramp_lag, load_share, system_load, corridor_order, corridor_buses, corridor_owner, corridor_row, corridor_ratio):
    horizon = plan.shape[1]
    padded = jnp.pad(plan, ((0, 0), (WMAX, 0)))
    held_mean = jnp.zeros(plan.shape, jnp.float32)
    lagged = jnp.zeros(plan.shape, jnp.float32)
    inverse = 1.0 / min_up.astype(jnp.float32)
    for offset in range(WMAX):
        shifted = padded[:, WMAX - offset:WMAX - offset + horizon]
        held_mean = held_mean + shifted * jnp.where(offset < min_up, inverse, 0.0)[:, None]
        lagged = lagged + shifted * (ramp_lag == offset).astype(jnp.float32)[:, None]
    dispatch = held_mean + ramp_gain * (plan - lagged)
    columns = jnp.take(ptdf_rows, unit_bus, axis=1)
    gen_flows = jnp.dot(columns, dispatch, preferred_element_type=jnp.float32, precision=lax.Precision.HIGHEST)
    load_flows = jnp.dot(ptdf_rows, load_share, preferred_element_type=jnp.float32, precision=lax.Precision.HIGHEST)
    base = gen_flows - load_flows[:, None] * system_load[None, :]
    coeff_list = []
    sens_list = []
    shift_list = []
    for step in range(NC):
        chosen = corridor_order[step]
        bus_from = corridor_buses[chosen, 0]
        bus_to = corridor_buses[chosen, 1]
        ratio = corridor_ratio[chosen]
        line_index = corridor_owner[chosen] * L_DEV + corridor_row[chosen]
        coefficient = ptdf_rows[:, bus_from] - ptdf_rows[:, bus_to]
        current = ptdf_rows[line_index]
        line_flow = base[line_index]
        for prior in range(step):
            coefficient = coefficient - coeff_list[prior] * (sens_list[prior][bus_from] - sens_list[prior][bus_to])
            current = current - coeff_list[prior][line_index] * sens_list[prior]
            line_flow = line_flow - coeff_list[prior][line_index] * shift_list[prior]
        weight = ratio / (1.0 + ratio * jnp.abs(current[bus_from] - current[bus_to]))
        coeff_list.append(coefficient)
        sens_list.append(weight * current)
        shift_list.append(weight * line_flow)
    flows = base
    for step in range(NC):
        flows = flows - coeff_list[step][:, None] * shift_list[step][None, :]
    return flows, jnp.stack(sens_list)
```

```python
import jax
import jax.numpy as jnp
from jax import lax
from jax.sharding import Mesh
from jax.sharding import PartitionSpec as P

WMAX = 24
NC = 4
LINE = ("line_0", "line_1", "line_2")
SNAP_LINE = ("snap", "line_0", "line_1", "line_2")


ramp_gain = 0.5


def body(
    ptdf_rows,
    plan,
    unit_bus,
    min_up,
    ramp_lag,
    load_share,
    system_load,
    corridor_order,
    corridor_buses,
    corridor_owner,
    corridor_row,
    corridor_ratio,
):
    unit_count, horizon = plan.shape
    snap_count = lax.axis_size("snap")
    line_count = lax.axis_size(LINE)
    here = lax.axis_index(LINE)

    picked_rows = []
    for step in range(NC):
        chosen = corridor_order[step]
        row = lax.dynamic_index_in_dim(ptdf_rows, corridor_row[chosen], 0, keepdims=False)
        picked_rows.append(jnp.where(corridor_owner[chosen] == here, row, 0.0))
    all_rows = lax.psum(jnp.stack(picked_rows), LINE)

    padded = jnp.pad(plan, ((0, 0), (WMAX, 0)))
    inverse = 1.0 / min_up.astype(jnp.float32)
    held_mean = jnp.zeros(plan.shape, jnp.float32)
    lagged = jnp.zeros(plan.shape, jnp.float32)
    for offset in range(WMAX):
        shifted = padded[:, WMAX - offset : WMAX - offset + horizon]
        held_mean = held_mean + shifted * jnp.where(offset < min_up, inverse, 0.0)[:, None]
        lagged = lagged + shifted * (ramp_lag == offset).astype(jnp.float32)[:, None]
    dispatch = held_mean + ramp_gain * (plan - lagged)
    unit_blocks = lax.all_to_all(dispatch, "snap", split_axis=1, concat_axis=0, tiled=True)
    everyone = lax.all_gather(unit_blocks, LINE, axis=0, tiled=True)

    order_ids = unit_bus.reshape(snap_count, line_count, unit_count).transpose(1, 0, 2).reshape(-1)
    columns = jnp.concatenate(
        [jnp.take(ptdf_rows, order_ids, axis=1), jnp.take(all_rows, order_ids, axis=1)], axis=0
    )
    load_flows = jnp.dot(
        ptdf_rows, load_share, preferred_element_type=jnp.float32, precision=lax.Precision.HIGHEST
    )
    row_load_flows = jnp.dot(
        all_rows, load_share, preferred_element_type=jnp.float32, precision=lax.Precision.HIGHEST
    )

    sens_list = []
    weights = []
    row_coeff_list = []
    ends_list = []
    for step in range(NC):
        chosen = corridor_order[step]
        bus_from = corridor_buses[chosen, 0]
        bus_to = corridor_buses[chosen, 1]
        ratio = corridor_ratio[chosen]
        initial = all_rows[step]
        row_coeffs = []
        for prior in range(step):
            prior_from, prior_to = ends_list[prior]
            value = initial[prior_from] - initial[prior_to]
            for earlier in range(prior):
                value = value - row_coeffs[earlier] * (
                    sens_list[earlier][prior_from] - sens_list[earlier][prior_to]
                )
            row_coeffs.append(value)
        current = initial
        for prior in range(step):
            current = current - row_coeffs[prior] * sens_list[prior]
        weight = ratio / (1.0 + ratio * jnp.abs(current[bus_from] - current[bus_to]))
        sens_list.append(weight * current)
        weights.append(weight)
        row_coeff_list.append(row_coeffs)
        ends_list.append((bus_from, bus_to))

    coeff_list = []
    for step in range(NC):
        bus_from, bus_to = ends_list[step]
        coefficient = ptdf_rows[:, bus_from] - ptdf_rows[:, bus_to]
        for prior in range(step):
            coefficient = coefficient - coeff_list[prior] * (
                sens_list[prior][bus_from] - sens_list[prior][bus_to]
            )
        coeff_list.append(coefficient)

    flows_all = jnp.dot(
        columns,
        everyone,
        preferred_element_type=jnp.float32,
        precision=lax.Precision.HIGHEST,
    )
    lines_here = ptdf_rows.shape[0]
    base = flows_all[:lines_here] - load_flows[:, None] * system_load[None, :]
    row_base = flows_all[lines_here:] - row_load_flows[:, None] * system_load[None, :]

    shift_list = []
    for step in range(NC):
        line_flow = row_base[step]
        for prior in range(step):
            line_flow = line_flow - row_coeff_list[step][prior] * shift_list[prior]
        shift_list.append(weights[step] * line_flow)
    flows = base
    for step in range(NC):
        flows = flows - coeff_list[step][:, None] * shift_list[step][None, :]
    return (flows, jnp.stack(sens_list))


def solution(mesh):
    torus = Mesh(
        mesh.devices.reshape(mesh.shape["snap"], 8, 4, 2), ("snap", "line_0", "line_1", "line_2")
    )
    in_specs = (
        P(LINE, None),
        P(SNAP_LINE, None),
        P(),
        P(SNAP_LINE),
        P(SNAP_LINE),
        P(),
        P("snap"),
        P(),
        P(),
        P(),
        P(),
        P(),
    )
    out_specs = (P(LINE, "snap"), P())
    return jax.shard_map(body, mesh=torus, in_specs=in_specs, out_specs=out_specs, check_vma=False)
```

```python
import jax
import jax.numpy as jnp
from jax import lax
from jax.sharding import Mesh
from jax.sharding import PartitionSpec as P

WMAX = 24
NC = 4
LINE = ("line_0", "line_1", "line_2")
SNAP_LINE = ("snap", "line_0", "line_1", "line_2")
HI = lax.Precision.HIGHEST


ramp_gain = 0.5


def line_total(x):
    for axis in ("line_2", "line_1", "line_0"):
        size = lax.axis_size(axis)
        step = 1
        while step < size:
            x = x + lax.ppermute(x, axis, [(i, i ^ step) for i in range(size)])
            step *= 2
    return x


def body(
    ptdf_rows,
    plan,
    unit_bus,
    min_up,
    ramp_lag,
    load_share,
    system_load,
    corridor_order,
    corridor_buses,
    corridor_owner,
    corridor_row,
    corridor_ratio,
):
    unit_count, horizon = plan.shape
    lines_here, buses = ptdf_rows.shape
    snap_count = lax.axis_size("snap")
    line_count = lax.axis_size(LINE)
    here = lax.axis_index(LINE)

    rows_of = corridor_row[corridor_order]
    mine = corridor_owner[corridor_order] == here
    ends = corridor_buses[corridor_order].reshape(-1)
    ratios = corridor_ratio[corridor_order]
    pick = jnp.where(
        mine[:, None] & (rows_of[:, None] == jnp.arange(lines_here)[None, :]), 1.0, 0.0
    )

    all_rows = line_total(jnp.dot(pick, ptdf_rows, precision=HI))

    padded = jnp.pad(plan, ((0, 0), (WMAX, 0)))
    inverse = 1.0 / min_up.astype(jnp.float32)
    held_mean = jnp.zeros(plan.shape, jnp.float32)
    lagged = jnp.zeros(plan.shape, jnp.float32)
    for offset in range(WMAX):
        shifted = padded[:, WMAX - offset : WMAX - offset + horizon]
        held_mean = held_mean + shifted * jnp.where(offset < min_up, inverse, 0.0)[:, None]
        lagged = lagged + shifted * (ramp_lag == offset).astype(jnp.float32)[:, None]
    dispatch = held_mean + ramp_gain * (plan - lagged)
    unit_blocks = lax.all_to_all(dispatch, "snap", split_axis=1, concat_axis=0, tiled=True)
    everyone = lax.all_gather(unit_blocks, LINE, axis=0, tiled=True)

    order_ids = unit_bus.reshape(snap_count, line_count, unit_count).transpose(1, 0, 2).reshape(-1)
    columns = jnp.take(ptdf_rows, order_ids, axis=1)
    row_columns = line_total(jnp.dot(pick, columns, precision=HI))

    probes = jnp.concatenate(
        [
            load_share[:, None],
            jnp.where(jnp.arange(buses)[:, None] == ends[None, :], 1.0, 0.0),
        ],
        axis=1,
    )
    local_probe = jnp.dot(ptdf_rows, probes, preferred_element_type=jnp.float32, precision=HI)
    row_probe = jnp.dot(all_rows, probes, preferred_element_type=jnp.float32, precision=HI)
    load_flows = local_probe[:, 0]
    at_ends = local_probe[:, 1:]
    row_load_flows = row_probe[:, 0]
    row_at_ends = row_probe[:, 1:]

    sens_ends = []
    weights = []
    row_coeff_list = []
    for step in range(NC):
        initial = row_at_ends[step]
        row_coeffs = []
        for prior in range(step):
            value = initial[2 * prior] - initial[2 * prior + 1]
            for earlier in range(prior):
                value = value - row_coeffs[earlier] * (
                    sens_ends[earlier][2 * prior] - sens_ends[earlier][2 * prior + 1]
                )
            row_coeffs.append(value)
        current = initial
        for prior in range(step):
            current = current - row_coeffs[prior] * sens_ends[prior]
        ratio = ratios[step]
        weight = ratio / (1.0 + ratio * jnp.abs(current[2 * step] - current[2 * step + 1]))
        sens_ends.append(weight * current)
        weights.append(weight)
        row_coeff_list.append(row_coeffs)

    sens_list = []
    for step in range(NC):
        current = all_rows[step]
        for prior in range(step):
            current = current - row_coeff_list[step][prior] * sens_list[prior]
        sens_list.append(weights[step] * current)

    coeff_list = []
    for step in range(NC):
        coefficient = at_ends[:, 2 * step] - at_ends[:, 2 * step + 1]
        for prior in range(step):
            coefficient = coefficient - coeff_list[prior] * (
                sens_ends[prior][2 * step] - sens_ends[prior][2 * step + 1]
            )
        coeff_list.append(coefficient)

    flows_all = jnp.dot(
        jnp.concatenate([columns, row_columns], axis=0),
        everyone,
        preferred_element_type=jnp.float32,
        precision=HI,
    )
    base = flows_all[:lines_here] - load_flows[:, None] * system_load[None, :]
    row_base = flows_all[lines_here:] - row_load_flows[:, None] * system_load[None, :]

    shift_list = []
    for step in range(NC):
        line_flow = row_base[step]
        for prior in range(step):
            line_flow = line_flow - row_coeff_list[step][prior] * shift_list[prior]
        shift_list.append(weights[step] * line_flow)
    flows = base
    for step in range(NC):
        flows = flows - coeff_list[step][:, None] * shift_list[step][None, :]
    return (flows, jnp.stack(sens_list))


def solution(mesh):
    torus = Mesh(
        mesh.devices.reshape(mesh.shape["snap"], 8, 4, 2), ("snap", "line_0", "line_1", "line_2")
    )
    in_specs = (
        P(LINE, None),
        P(SNAP_LINE, None),
        P(),
        P(SNAP_LINE),
        P(SNAP_LINE),
        P(),
        P("snap"),
        P(),
        P(),
        P(),
        P(),
        P(),
    )
    out_specs = (P(LINE, "snap"), P())
    return jax.shard_map(body, mesh=torus, in_specs=in_specs, out_specs=out_specs, check_vma=False)
```

```python
import jax
import jax.numpy as jnp
from jax import lax
from jax.sharding import Mesh
from jax.sharding import PartitionSpec as P

WMAX = 24
NC = 4
LINE = ("line_0", "line_1", "line_2")
SNAP_LINE = ("snap", "line_0", "line_1", "line_2")
HI = lax.Precision.HIGHEST
STAGES = (("line_2", 1), ("line_1", 1), ("line_1", 2), ("line_0", 1), ("line_0", 2), ("line_0", 4))


ramp_gain = 0.5


def line_total(x):
    for axis, step in STAGES:
        size = lax.axis_size(axis)
        x = x + lax.ppermute(x, axis, [(i, i ^ step) for i in range(size)])
    return x


def line_scatter(x):
    for axis, step in STAGES:
        size = lax.axis_size(axis)
        upper = (lax.axis_index(axis) // step) % 2 == 1
        half = x.shape[1] // 2
        keep = jnp.where(upper, x[:, half:], x[:, :half])
        give = jnp.where(upper, x[:, :half], x[:, half:])
        x = keep + lax.ppermute(give, axis, [(i, i ^ step) for i in range(size)])
    return x


def piece_order(sizes):
    line_0, line_1, line_2 = sizes
    slice_of = []
    for i in range(line_0 * line_1 * line_2):
        digits = {"line_0": i // (line_1 * line_2), "line_1": (i // line_2) % line_1, "line_2": i % line_2}
        s = 0
        for axis, step in STAGES:
            s = s * 2 + (digits[axis] // step) % 2
        slice_of.append(s)
    owner_of = [0] * len(slice_of)
    for i, s in enumerate(slice_of):
        owner_of[s] = i
    return owner_of


def body(
    ptdf_rows,
    plan,
    unit_bus,
    min_up,
    ramp_lag,
    load_share,
    system_load,
    corridor_order,
    corridor_buses,
    corridor_owner,
    corridor_row,
    corridor_ratio,
):
    unit_count, horizon = plan.shape
    lines_here, buses = ptdf_rows.shape
    snap_count = lax.axis_size("snap")
    line_count = lax.axis_size(LINE)
    here = lax.axis_index(LINE)

    rows_of = corridor_row[corridor_order]
    mine = corridor_owner[corridor_order] == here
    ends = corridor_buses[corridor_order].reshape(-1)
    ratios = corridor_ratio[corridor_order]
    pick = jnp.where(
        mine[:, None] & (rows_of[:, None] == jnp.arange(lines_here)[None, :]), 1.0, 0.0
    )

    row_piece = line_scatter(jnp.dot(pick, ptdf_rows, precision=HI))
    piece_width = row_piece.shape[1]
    packed = row_piece.reshape(-1)
    block_width = horizon // snap_count
    extra_rows = -(-packed.shape[0] // block_width)
    extra_rows += -(unit_count * snap_count + extra_rows) % 8
    packed = jnp.pad(packed, (0, extra_rows * block_width - packed.shape[0])).reshape(extra_rows, block_width)

    padded = jnp.pad(plan, ((0, 0), (WMAX, 0)))
    inverse = 1.0 / min_up.astype(jnp.float32)
    held_mean = jnp.zeros(plan.shape, jnp.float32)
    lagged = jnp.zeros(plan.shape, jnp.float32)
    for offset in range(WMAX):
        shifted = padded[:, WMAX - offset : WMAX - offset + horizon]
        held_mean = held_mean + shifted * jnp.where(offset < min_up, inverse, 0.0)[:, None]
        lagged = lagged + shifted * (ramp_lag == offset).astype(jnp.float32)[:, None]
    dispatch = held_mean + ramp_gain * (plan - lagged)
    unit_blocks = lax.all_to_all(dispatch, "snap", split_axis=1, concat_axis=0, tiled=True)
    block_units = unit_blocks.shape[0]
    everyone = lax.all_gather(
        jnp.concatenate([unit_blocks, packed], axis=0), LINE, axis=0, tiled=True
    )

    order_ids = unit_bus.reshape(snap_count, line_count, unit_count).transpose(1, 0, 2).reshape(-1)
    columns = jnp.take(ptdf_rows, order_ids, axis=1).reshape(lines_here, line_count, block_units)
    columns = jnp.pad(columns, ((0, 0), (0, 0), (0, extra_rows))).reshape(lines_here, -1)

    probes = jnp.concatenate(
        [
            load_share[:, None],
            jnp.where(jnp.arange(buses)[:, None] == ends[None, :], 1.0, 0.0),
        ],
        axis=1,
    )
    local_probe = jnp.dot(ptdf_rows, probes, preferred_element_type=jnp.float32, precision=HI)
    row_probe = line_total(jnp.dot(pick, local_probe, precision=HI))
    load_flows = local_probe[:, 0]
    at_ends = local_probe[:, 1:]
    row_at_ends = row_probe[:, 1:]

    sens_ends = []
    weights = []
    row_coeff_list = []
    for step in range(NC):
        initial = row_at_ends[step]
        row_coeffs = []
        for prior in range(step):
            value = initial[2 * prior] - initial[2 * prior + 1]
            for earlier in range(prior):
                value = value - row_coeffs[earlier] * (
                    sens_ends[earlier][2 * prior] - sens_ends[earlier][2 * prior + 1]
                )
            row_coeffs.append(value)
        current = initial
        for prior in range(step):
            current = current - row_coeffs[prior] * sens_ends[prior]
        ratio = ratios[step]
        weight = ratio / (1.0 + ratio * jnp.abs(current[2 * step] - current[2 * step + 1]))
        sens_ends.append(weight * current)
        weights.append(weight)
        row_coeff_list.append(row_coeffs)

    coeff_list = []
    for step in range(NC):
        coefficient = at_ends[:, 2 * step] - at_ends[:, 2 * step + 1]
        for prior in range(step):
            coefficient = coefficient - coeff_list[prior] * (
                sens_ends[prior][2 * step] - sens_ends[prior][2 * step + 1]
            )
        coeff_list.append(coefficient)

    gen_flows = jnp.dot(columns, everyone, preferred_element_type=jnp.float32, precision=HI)
    base = gen_flows - load_flows[:, None] * system_load[None, :]
    row_base = line_total(jnp.dot(pick, base, precision=HI))

    pieces = everyone.reshape(line_count, block_units + extra_rows, block_width)[:, block_units:]
    pieces = pieces.reshape(line_count, -1)[:, : NC * piece_width].reshape(line_count, NC, piece_width)
    pieces = jnp.take(pieces, jnp.array(piece_order([lax.axis_size(a) for a in LINE])), axis=0)
    all_rows = pieces.transpose(1, 0, 2).reshape(NC, buses)

    sens_list = []
    for step in range(NC):
        current = all_rows[step]
        for prior in range(step):
            current = current - row_coeff_list[step][prior] * sens_list[prior]
        sens_list.append(weights[step] * current)

    shift_list = []
    for step in range(NC):
        line_flow = row_base[step]
        for prior in range(step):
            line_flow = line_flow - row_coeff_list[step][prior] * shift_list[prior]
        shift_list.append(weights[step] * line_flow)
    flows = base
    for step in range(NC):
        flows = flows - coeff_list[step][:, None] * shift_list[step][None, :]
    return (flows, jnp.stack(sens_list))


def solution(mesh):
    torus = Mesh(
        mesh.devices.reshape(mesh.shape["snap"], 8, 4, 2), ("snap", "line_0", "line_1", "line_2")
    )
    in_specs = (
        P(LINE, None),
        P(SNAP_LINE, None),
        P(),
        P(SNAP_LINE),
        P(SNAP_LINE),
        P(),
        P("snap"),
        P(),
        P(),
        P(),
        P(),
        P(),
    )
    out_specs = (P(LINE, "snap"), P())
    return jax.shard_map(body, mesh=torus, in_specs=in_specs, out_specs=out_specs, check_vma=False)
```

```python
import jax
import jax.numpy as jnp
from jax import lax
from jax.sharding import Mesh
from jax.sharding import PartitionSpec as P

WMAX = 24
NC = 4
LINE = ("line_0", "line_1", "line_2")
SNAP_LINE = ("snap", "line_0", "line_1", "line_2")
HI = lax.Precision.HIGHEST
STAGES = (("line_2", 1), ("line_1", 1), ("line_1", 2), ("line_0", 1), ("line_0", 2), ("line_0", 4))


ramp_gain = 0.5


def line_total(x):
    for axis, step in STAGES:
        size = lax.axis_size(axis)
        x = x + lax.ppermute(x, axis, [(i, i ^ step) for i in range(size)])
    return x


def line_scatter(x):
    for axis, step in STAGES:
        size = lax.axis_size(axis)
        upper = (lax.axis_index(axis) // step) % 2 == 1
        half = x.shape[1] // 2
        keep = jnp.where(upper, x[:, half:], x[:, :half])
        give = jnp.where(upper, x[:, :half], x[:, half:])
        x = keep + lax.ppermute(give, axis, [(i, i ^ step) for i in range(size)])
    return x


def piece_order(sizes):
    line_0, line_1, line_2 = sizes
    slice_of = []
    for i in range(line_0 * line_1 * line_2):
        digits = {"line_0": i // (line_1 * line_2), "line_1": (i // line_2) % line_1, "line_2": i % line_2}
        s = 0
        for axis, step in STAGES:
            s = s * 2 + (digits[axis] // step) % 2
        slice_of.append(s)
    owner_of = [0] * len(slice_of)
    for i, s in enumerate(slice_of):
        owner_of[s] = i
    return owner_of


def body(
    ptdf_rows,
    plan,
    unit_bus,
    min_up,
    ramp_lag,
    load_share,
    system_load,
    corridor_order,
    corridor_buses,
    corridor_owner,
    corridor_row,
    corridor_ratio,
):
    unit_count, horizon = plan.shape
    lines_here, buses = ptdf_rows.shape
    snap_count = lax.axis_size("snap")
    line_count = lax.axis_size(LINE)
    here = lax.axis_index(LINE)

    rows_of = corridor_row[corridor_order]
    mine = corridor_owner[corridor_order] == here
    ends = corridor_buses[corridor_order].reshape(-1)
    ratios = corridor_ratio[corridor_order]
    pick = jnp.where(
        mine[:, None] & (rows_of[:, None] == jnp.arange(lines_here)[None, :]), 1.0, 0.0
    )

    padded = jnp.pad(plan, ((0, 0), (WMAX, 0)))
    inverse = 1.0 / min_up.astype(jnp.float32)
    held_mean = jnp.zeros(plan.shape, jnp.float32)
    lagged = jnp.zeros(plan.shape, jnp.float32)
    for offset in range(WMAX):
        shifted = padded[:, WMAX - offset : WMAX - offset + horizon]
        held_mean = held_mean + shifted * jnp.where(offset < min_up, inverse, 0.0)[:, None]
        lagged = lagged + shifted * (ramp_lag == offset).astype(jnp.float32)[:, None]
    dispatch = held_mean + ramp_gain * (plan - lagged)
    unit_blocks = lax.all_to_all(dispatch, "snap", split_axis=1, concat_axis=0, tiled=True)

    dispatch, pick = lax.optimization_barrier((dispatch, pick))
    row_piece = line_scatter(jnp.dot(pick, ptdf_rows, precision=HI))
    piece_width = row_piece.shape[1]
    packed = row_piece.reshape(-1)
    block_width = horizon // snap_count
    extra_rows = -(-packed.shape[0] // block_width)
    extra_rows += -(unit_count * snap_count + extra_rows) % 8
    packed = jnp.pad(packed, (0, extra_rows * block_width - packed.shape[0])).reshape(extra_rows, block_width)
    block_units = unit_blocks.shape[0]
    everyone = lax.all_gather(
        jnp.concatenate([unit_blocks, packed], axis=0), LINE, axis=0, tiled=True
    )

    order_ids = unit_bus.reshape(snap_count, line_count, unit_count).transpose(1, 0, 2).reshape(-1)
    columns = jnp.take(ptdf_rows, order_ids, axis=1).reshape(lines_here, line_count, block_units)
    columns = jnp.pad(columns, ((0, 0), (0, 0), (0, extra_rows))).reshape(lines_here, -1)

    probes = jnp.concatenate(
        [
            load_share[:, None],
            jnp.where(jnp.arange(buses)[:, None] == ends[None, :], 1.0, 0.0),
        ],
        axis=1,
    )
    local_probe = jnp.dot(ptdf_rows, probes, preferred_element_type=jnp.float32, precision=HI)
    row_probe = line_total(jnp.dot(pick, local_probe, precision=HI))
    load_flows = local_probe[:, 0]
    at_ends = local_probe[:, 1:]
    row_at_ends = row_probe[:, 1:]

    sens_ends = []
    weights = []
    row_coeff_list = []
    for step in range(NC):
        initial = row_at_ends[step]
        row_coeffs = []
        for prior in range(step):
            value = initial[2 * prior] - initial[2 * prior + 1]
            for earlier in range(prior):
                value = value - row_coeffs[earlier] * (
                    sens_ends[earlier][2 * prior] - sens_ends[earlier][2 * prior + 1]
                )
            row_coeffs.append(value)
        current = initial
        for prior in range(step):
            current = current - row_coeffs[prior] * sens_ends[prior]
        ratio = ratios[step]
        weight = ratio / (1.0 + ratio * jnp.abs(current[2 * step] - current[2 * step + 1]))
        sens_ends.append(weight * current)
        weights.append(weight)
        row_coeff_list.append(row_coeffs)

    coeff_list = []
    for step in range(NC):
        coefficient = at_ends[:, 2 * step] - at_ends[:, 2 * step + 1]
        for prior in range(step):
            coefficient = coefficient - coeff_list[prior] * (
                sens_ends[prior][2 * step] - sens_ends[prior][2 * step + 1]
            )
        coeff_list.append(coefficient)

    gen_flows = jnp.dot(columns, everyone, preferred_element_type=jnp.float32, precision=HI)
    base = gen_flows - load_flows[:, None] * system_load[None, :]
    row_base = line_total(jnp.dot(pick, base, precision=HI))

    pieces = everyone.reshape(line_count, block_units + extra_rows, block_width)[:, block_units:]
    pieces = pieces.reshape(line_count, -1)[:, : NC * piece_width].reshape(line_count, NC, piece_width)
    pieces = jnp.take(pieces, jnp.array(piece_order([lax.axis_size(a) for a in LINE])), axis=0)
    all_rows = pieces.transpose(1, 0, 2).reshape(NC, buses)

    sens_list = []
    for step in range(NC):
        current = all_rows[step]
        for prior in range(step):
            current = current - row_coeff_list[step][prior] * sens_list[prior]
        sens_list.append(weights[step] * current)

    shift_list = []
    for step in range(NC):
        line_flow = row_base[step]
        for prior in range(step):
            line_flow = line_flow - row_coeff_list[step][prior] * shift_list[prior]
        shift_list.append(weights[step] * line_flow)
    flows = base
    for step in range(NC):
        flows = flows - coeff_list[step][:, None] * shift_list[step][None, :]
    return (flows, jnp.stack(sens_list))


def solution(mesh):
    torus = Mesh(
        mesh.devices.reshape(mesh.shape["snap"], 8, 4, 2), ("snap", "line_0", "line_1", "line_2")
    )
    in_specs = (
        P(LINE, None),
        P(SNAP_LINE, None),
        P(),
        P(SNAP_LINE),
        P(SNAP_LINE),
        P(),
        P("snap"),
        P(),
        P(),
        P(),
        P(),
        P(),
    )
    out_specs = (P(LINE, "snap"), P())
    return jax.shard_map(body, mesh=torus, in_specs=in_specs, out_specs=out_specs, check_vma=False)
```

```python
import jax
import jax.numpy as jnp
from jax import lax
from jax.sharding import Mesh
from jax.sharding import PartitionSpec as P

WMAX = 24
NC = 4
LINE = ("line_0", "line_1", "line_2")
SNAP_LINE = ("snap", "line_0", "line_1", "line_2")
HI = lax.Precision.HIGHEST
STAGES = (("line_2", 1), ("line_1", 1), ("line_1", 2), ("line_0", 1), ("line_0", 2), ("line_0", 4))


ramp_gain = 0.5


def line_total(x):
    for axis, step in STAGES:
        size = lax.axis_size(axis)
        x = x + lax.ppermute(x, axis, [(i, i ^ step) for i in range(size)])
    return x


def line_scatter(x):
    for axis, step in STAGES:
        size = lax.axis_size(axis)
        upper = (lax.axis_index(axis) // step) % 2 == 1
        half = x.shape[1] // 2
        keep = jnp.where(upper, x[:, half:], x[:, :half])
        give = jnp.where(upper, x[:, :half], x[:, half:])
        x = keep + lax.ppermute(give, axis, [(i, i ^ step) for i in range(size)])
    return x


def piece_order(sizes):
    line_0, line_1, line_2 = sizes
    slice_of = []
    for i in range(line_0 * line_1 * line_2):
        digits = {"line_0": i // (line_1 * line_2), "line_1": (i // line_2) % line_1, "line_2": i % line_2}
        s = 0
        for axis, step in STAGES:
            s = s * 2 + (digits[axis] // step) % 2
        slice_of.append(s)
    owner_of = [0] * len(slice_of)
    for i, s in enumerate(slice_of):
        owner_of[s] = i
    return owner_of


def body(
    ptdf_rows,
    plan,
    unit_bus,
    min_up,
    ramp_lag,
    load_share,
    system_load,
    corridor_order,
    corridor_buses,
    corridor_owner,
    corridor_row,
    corridor_ratio,
):
    unit_count, horizon = plan.shape
    lines_here, buses = ptdf_rows.shape
    snap_count = lax.axis_size("snap")
    line_count = lax.axis_size(LINE)
    here = lax.axis_index(LINE)

    rows_of = corridor_row[corridor_order]
    mine = corridor_owner[corridor_order] == here
    ends = corridor_buses[corridor_order].reshape(-1)
    ratios = corridor_ratio[corridor_order]
    pick = jnp.where(
        mine[:, None] & (rows_of[:, None] == jnp.arange(lines_here)[None, :]), 1.0, 0.0
    )

    row_piece = line_scatter(jnp.where(mine[:, None], jnp.take(ptdf_rows, rows_of, axis=0), 0.0))
    piece_width = row_piece.shape[1]
    packed = row_piece.reshape(-1)
    block_width = horizon // snap_count
    extra_rows = -(-packed.shape[0] // block_width)
    extra_rows += -(unit_count * snap_count + extra_rows) % 8
    packed = jnp.pad(packed, (0, extra_rows * block_width - packed.shape[0])).reshape(extra_rows, block_width)

    padded = jnp.pad(plan, ((0, 0), (WMAX, 0)))
    inverse = 1.0 / min_up.astype(jnp.float32)
    held_mean = jnp.zeros(plan.shape, jnp.float32)
    lagged = jnp.zeros(plan.shape, jnp.float32)
    for offset in range(WMAX):
        shifted = padded[:, WMAX - offset : WMAX - offset + horizon]
        held_mean = held_mean + shifted * jnp.where(offset < min_up, inverse, 0.0)[:, None]
        lagged = lagged + shifted * (ramp_lag == offset).astype(jnp.float32)[:, None]
    dispatch = held_mean + ramp_gain * (plan - lagged)
    unit_blocks = lax.all_to_all(dispatch, "snap", split_axis=1, concat_axis=0, tiled=True)
    block_units = unit_blocks.shape[0]
    everyone = lax.all_gather(
        jnp.concatenate([unit_blocks, packed], axis=0), LINE, axis=0, tiled=True
    )

    order_ids = unit_bus.reshape(snap_count, line_count, unit_count).transpose(1, 0, 2).reshape(-1)
    columns = jnp.take(ptdf_rows, order_ids, axis=1).reshape(lines_here, line_count, block_units)
    columns = jnp.pad(columns, ((0, 0), (0, 0), (0, extra_rows))).reshape(lines_here, -1)

    probes = jnp.concatenate(
        [
            load_share[:, None],
            jnp.where(jnp.arange(buses)[:, None] == ends[None, :], 1.0, 0.0),
        ],
        axis=1,
    )
    local_probe = jnp.dot(ptdf_rows, probes, preferred_element_type=jnp.float32, precision=HI)
    row_probe = line_total(jnp.dot(pick, local_probe, precision=HI))
    load_flows = local_probe[:, 0]
    at_ends = local_probe[:, 1:]
    row_at_ends = row_probe[:, 1:]

    sens_ends = []
    weights = []
    row_coeff_list = []
    for step in range(NC):
        initial = row_at_ends[step]
        row_coeffs = []
        for prior in range(step):
            value = initial[2 * prior] - initial[2 * prior + 1]
            for earlier in range(prior):
                value = value - row_coeffs[earlier] * (
                    sens_ends[earlier][2 * prior] - sens_ends[earlier][2 * prior + 1]
                )
            row_coeffs.append(value)
        current = initial
        for prior in range(step):
            current = current - row_coeffs[prior] * sens_ends[prior]
        ratio = ratios[step]
        weight = ratio / (1.0 + ratio * jnp.abs(current[2 * step] - current[2 * step + 1]))
        sens_ends.append(weight * current)
        weights.append(weight)
        row_coeff_list.append(row_coeffs)

    coeff_list = []
    for step in range(NC):
        coefficient = at_ends[:, 2 * step] - at_ends[:, 2 * step + 1]
        for prior in range(step):
            coefficient = coefficient - coeff_list[prior] * (
                sens_ends[prior][2 * step] - sens_ends[prior][2 * step + 1]
            )
        coeff_list.append(coefficient)

    gen_flows = jnp.dot(columns, everyone, preferred_element_type=jnp.float32, precision=HI)
    base = gen_flows - load_flows[:, None] * system_load[None, :]
    row_base = line_total(jnp.dot(pick, base, precision=HI))

    pieces = everyone.reshape(line_count, block_units + extra_rows, block_width)[:, block_units:]
    pieces = pieces.reshape(line_count, -1)[:, : NC * piece_width].reshape(line_count, NC, piece_width)
    pieces = jnp.take(pieces, jnp.array(piece_order([lax.axis_size(a) for a in LINE])), axis=0)
    all_rows = pieces.transpose(1, 0, 2).reshape(NC, buses)

    sens_list = []
    for step in range(NC):
        current = all_rows[step]
        for prior in range(step):
            current = current - row_coeff_list[step][prior] * sens_list[prior]
        sens_list.append(weights[step] * current)

    shift_list = []
    for step in range(NC):
        line_flow = row_base[step]
        for prior in range(step):
            line_flow = line_flow - row_coeff_list[step][prior] * shift_list[prior]
        shift_list.append(weights[step] * line_flow)
    flows = base
    for step in range(NC):
        flows = flows - coeff_list[step][:, None] * shift_list[step][None, :]
    return (flows, jnp.stack(sens_list))


def solution(mesh):
    torus = Mesh(
        mesh.devices.reshape(mesh.shape["snap"], 8, 4, 2), ("snap", "line_0", "line_1", "line_2")
    )
    in_specs = (
        P(LINE, None),
        P(SNAP_LINE, None),
        P(),
        P(SNAP_LINE),
        P(SNAP_LINE),
        P(),
        P("snap"),
        P(),
        P(),
        P(),
        P(),
        P(),
    )
    out_specs = (P(LINE, "snap"), P())
    return jax.shard_map(body, mesh=torus, in_specs=in_specs, out_specs=out_specs, check_vma=False)
```

```python
import jax
import jax.numpy as jnp
from jax import lax
from jax.sharding import Mesh
from jax.sharding import PartitionSpec as P

WMAX = 24
NC = 4
LINE = ("line_0", "line_1", "line_2")
SNAP_LINE = ("snap", "line_0", "line_1", "line_2")
HI = lax.Precision.HIGHEST
STAGES = (("line_2", 1), ("line_1", 1), ("line_1", 2), ("line_0", 1), ("line_0", 2), ("line_0", 4))


ramp_gain = 0.5


def line_total(x):
    for axis, step in STAGES:
        size = lax.axis_size(axis)
        x = x + lax.ppermute(x, axis, [(i, i ^ step) for i in range(size)])
    return x


def line_total_wide(x):
    x = x + lax.ppermute(x, "line_2", [(i, i ^ 1) for i in range(lax.axis_size("line_2"))])
    chips = ("line_0", "line_1")
    count = lax.axis_size(chips)
    rows, width = x.shape
    parts = x.reshape(rows, count, width // count).transpose(1, 0, 2)
    mine = lax.all_to_all(parts, chips, 0, 0, tiled=True).sum(axis=0)
    spread = jnp.broadcast_to(mine[None], (count,) + mine.shape)
    whole = lax.all_to_all(spread, chips, 0, 0, tiled=True)
    return whole.transpose(1, 0, 2).reshape(rows, width)


def line_scatter(x):
    upper = lax.axis_index("line_2") == 1
    half = x.shape[1] // 2
    keep = jnp.where(upper, x[:, half:], x[:, :half])
    give = jnp.where(upper, x[:, :half], x[:, half:])
    x = keep + lax.ppermute(give, "line_2", [(i, i ^ 1) for i in range(lax.axis_size("line_2"))])
    chips = ("line_0", "line_1")
    count = lax.axis_size(chips)
    rows, width = x.shape
    parts = x.reshape(rows, count, width // count).transpose(1, 0, 2)
    return lax.all_to_all(parts, chips, 0, 0, tiled=True).sum(axis=0)


def piece_order(sizes):
    line_0, line_1, line_2 = sizes
    owner_of = [0] * (line_0 * line_1 * line_2)
    for i in range(len(owner_of)):
        digits = (i // (line_1 * line_2), (i // line_2) % line_1, i % line_2)
        owner_of[digits[2] * line_0 * line_1 + digits[0] * line_1 + digits[1]] = i
    return owner_of


def body(
    ptdf_rows,
    plan,
    unit_bus,
    min_up,
    ramp_lag,
    load_share,
    system_load,
    corridor_order,
    corridor_buses,
    corridor_owner,
    corridor_row,
    corridor_ratio,
):
    unit_count, horizon = plan.shape
    lines_here, buses = ptdf_rows.shape
    snap_count = lax.axis_size("snap")
    line_count = lax.axis_size(LINE)
    here = lax.axis_index(LINE)

    rows_of = corridor_row[corridor_order]
    mine = corridor_owner[corridor_order] == here
    ends = corridor_buses[corridor_order].reshape(-1)
    ratios = corridor_ratio[corridor_order]
    pick = jnp.where(
        mine[:, None] & (rows_of[:, None] == jnp.arange(lines_here)[None, :]), 1.0, 0.0
    )

    row_piece = line_scatter(jnp.where(mine[:, None], jnp.take(ptdf_rows, rows_of, axis=0), 0.0))
    piece_width = row_piece.shape[1]
    packed = row_piece.reshape(-1)
    block_width = horizon // snap_count
    extra_rows = -(-packed.shape[0] // block_width)
    extra_rows += -(unit_count * snap_count + extra_rows) % 8
    packed = jnp.pad(packed, (0, extra_rows * block_width - packed.shape[0])).reshape(extra_rows, block_width)

    padded = jnp.pad(plan, ((0, 0), (WMAX, 0)))
    inverse = 1.0 / min_up.astype(jnp.float32)
    held_mean = jnp.zeros(plan.shape, jnp.float32)
    lagged = jnp.zeros(plan.shape, jnp.float32)
    for offset in range(WMAX):
        shifted = padded[:, WMAX - offset : WMAX - offset + horizon]
        held_mean = held_mean + shifted * jnp.where(offset < min_up, inverse, 0.0)[:, None]
        lagged = lagged + shifted * (ramp_lag == offset).astype(jnp.float32)[:, None]
    dispatch = held_mean + ramp_gain * (plan - lagged)
    unit_blocks = lax.all_to_all(dispatch, "snap", split_axis=1, concat_axis=0, tiled=True)
    block_units = unit_blocks.shape[0]
    everyone = lax.all_gather(
        jnp.concatenate([unit_blocks, packed], axis=0), LINE, axis=0, tiled=True
    )

    order_ids = unit_bus.reshape(snap_count, line_count, unit_count).transpose(1, 0, 2).reshape(-1)
    columns = jnp.take(ptdf_rows, order_ids, axis=1).reshape(lines_here, line_count, block_units)
    columns = jnp.pad(columns, ((0, 0), (0, 0), (0, extra_rows))).reshape(lines_here, -1)

    probes = jnp.concatenate(
        [
            load_share[:, None],
            jnp.where(jnp.arange(buses)[:, None] == ends[None, :], 1.0, 0.0),
        ],
        axis=1,
    )
    local_probe = jnp.dot(ptdf_rows, probes, preferred_element_type=jnp.float32, precision=HI)
    row_probe = line_total(jnp.dot(pick, local_probe, precision=HI))
    load_flows = local_probe[:, 0]
    at_ends = local_probe[:, 1:]
    row_at_ends = row_probe[:, 1:]

    sens_ends = []
    weights = []
    row_coeff_list = []
    for step in range(NC):
        initial = row_at_ends[step]
        row_coeffs = []
        for prior in range(step):
            value = initial[2 * prior] - initial[2 * prior + 1]
            for earlier in range(prior):
                value = value - row_coeffs[earlier] * (
                    sens_ends[earlier][2 * prior] - sens_ends[earlier][2 * prior + 1]
                )
            row_coeffs.append(value)
        current = initial
        for prior in range(step):
            current = current - row_coeffs[prior] * sens_ends[prior]
        ratio = ratios[step]
        weight = ratio / (1.0 + ratio * jnp.abs(current[2 * step] - current[2 * step + 1]))
        sens_ends.append(weight * current)
        weights.append(weight)
        row_coeff_list.append(row_coeffs)

    coeff_list = []
    for step in range(NC):
        coefficient = at_ends[:, 2 * step] - at_ends[:, 2 * step + 1]
        for prior in range(step):
            coefficient = coefficient - coeff_list[prior] * (
                sens_ends[prior][2 * step] - sens_ends[prior][2 * step + 1]
            )
        coeff_list.append(coefficient)

    gen_flows = jnp.dot(columns, everyone, preferred_element_type=jnp.float32, precision=HI)
    base = gen_flows - load_flows[:, None] * system_load[None, :]
    row_base = line_total_wide(jnp.dot(pick, base, precision=HI))

    pieces = everyone.reshape(line_count, block_units + extra_rows, block_width)[:, block_units:]
    pieces = pieces.reshape(line_count, -1)[:, : NC * piece_width].reshape(line_count, NC, piece_width)
    pieces = jnp.take(pieces, jnp.array(piece_order([lax.axis_size(a) for a in LINE])), axis=0)
    all_rows = pieces.transpose(1, 0, 2).reshape(NC, buses)

    sens_list = []
    for step in range(NC):
        current = all_rows[step]
        for prior in range(step):
            current = current - row_coeff_list[step][prior] * sens_list[prior]
        sens_list.append(weights[step] * current)

    shift_list = []
    for step in range(NC):
        line_flow = row_base[step]
        for prior in range(step):
            line_flow = line_flow - row_coeff_list[step][prior] * shift_list[prior]
        shift_list.append(weights[step] * line_flow)
    flows = base
    for step in range(NC):
        flows = flows - coeff_list[step][:, None] * shift_list[step][None, :]
    return (flows, jnp.stack(sens_list))


def solution(mesh):
    torus = Mesh(
        mesh.devices.reshape(mesh.shape["snap"], 8, 4, 2), ("snap", "line_0", "line_1", "line_2")
    )
    in_specs = (
        P(LINE, None),
        P(SNAP_LINE, None),
        P(),
        P(SNAP_LINE),
        P(SNAP_LINE),
        P(),
        P("snap"),
        P(),
        P(),
        P(),
        P(),
        P(),
    )
    out_specs = (P(LINE, "snap"), P())
    return jax.shard_map(body, mesh=torus, in_specs=in_specs, out_specs=out_specs, check_vma=False)
```

```python
import jax
import jax.numpy as jnp
from jax import lax
from jax.sharding import Mesh
from jax.sharding import PartitionSpec as P

WMAX = 24
NC = 4
LINE = ("line_0", "line_1", "line_2")
SNAP_LINE = ("snap", "line_0", "line_1", "line_2")
HI = lax.Precision.HIGHEST


ramp_gain = 0.5


def line_total(x):
    for axis in ("line_2", "line_1", "line_0"):
        size = lax.axis_size(axis)
        total = x
        for shift in range(1, size):
            total = total + lax.ppermute(x, axis, [(i, (i + shift) % size) for i in range(size)])
        x = total
    return x


def line_total_pairs(x):
    for axis in ("line_2", "line_1", "line_0"):
        size = lax.axis_size(axis)
        step = 1
        while step < size:
            x = x + lax.ppermute(x, axis, [(i, i ^ step) for i in range(size)])
            step *= 2
    return x


def line_scatter(x):
    for axis in ("line_2", "line_1", "line_0"):
        size = lax.axis_size(axis)
        me = lax.axis_index(axis)
        rows, width = x.shape
        shares = x.reshape(rows, size, width // size)
        total = lax.dynamic_index_in_dim(shares, me, axis=1, keepdims=False)
        for shift in range(1, size):
            out = lax.dynamic_index_in_dim(shares, (me + shift) % size, axis=1, keepdims=False)
            total = total + lax.ppermute(out, axis, [(i, (i + shift) % size) for i in range(size)])
        x = total
    return x


def piece_order(sizes):
    line_0, line_1, line_2 = sizes
    owner_of = [0] * (line_0 * line_1 * line_2)
    for i in range(len(owner_of)):
        l0, l1, l2 = i // (line_1 * line_2), (i // line_2) % line_1, i % line_2
        owner_of[(l2 * line_1 + l1) * line_0 + l0] = i
    return owner_of


def body(
    ptdf_rows,
    plan,
    unit_bus,
    min_up,
    ramp_lag,
    load_share,
    system_load,
    corridor_order,
    corridor_buses,
    corridor_owner,
    corridor_row,
    corridor_ratio,
):
    unit_count, horizon = plan.shape
    lines_here, buses = ptdf_rows.shape
    snap_count = lax.axis_size("snap")
    line_count = lax.axis_size(LINE)
    here = lax.axis_index(LINE)

    rows_of = corridor_row[corridor_order]
    mine = corridor_owner[corridor_order] == here
    ends = corridor_buses[corridor_order].reshape(-1)
    ratios = corridor_ratio[corridor_order]
    pick = jnp.where(
        mine[:, None] & (rows_of[:, None] == jnp.arange(lines_here)[None, :]), 1.0, 0.0
    )

    row_piece = line_scatter(jnp.where(mine[:, None], jnp.take(ptdf_rows, rows_of, axis=0), 0.0))
    piece_width = row_piece.shape[1]
    packed = row_piece.reshape(-1)
    block_width = horizon // snap_count
    extra_rows = -(-packed.shape[0] // block_width)
    extra_rows += -(unit_count * snap_count + extra_rows) % 8
    packed = jnp.pad(packed, (0, extra_rows * block_width - packed.shape[0])).reshape(extra_rows, block_width)

    padded = jnp.pad(plan, ((0, 0), (WMAX, 0)))
    inverse = 1.0 / min_up.astype(jnp.float32)
    held_mean = jnp.zeros(plan.shape, jnp.float32)
    lagged = jnp.zeros(plan.shape, jnp.float32)
    for offset in range(WMAX):
        shifted = padded[:, WMAX - offset : WMAX - offset + horizon]
        held_mean = held_mean + shifted * jnp.where(offset < min_up, inverse, 0.0)[:, None]
        lagged = lagged + shifted * (ramp_lag == offset).astype(jnp.float32)[:, None]
    dispatch = held_mean + ramp_gain * (plan - lagged)
    unit_blocks = lax.all_to_all(dispatch, "snap", split_axis=1, concat_axis=0, tiled=True)
    block_units = unit_blocks.shape[0]
    everyone = lax.all_gather(
        jnp.concatenate([unit_blocks, packed], axis=0), LINE, axis=0, tiled=True
    )

    order_ids = unit_bus.reshape(snap_count, line_count, unit_count).transpose(1, 0, 2).reshape(-1)
    columns = jnp.take(ptdf_rows, order_ids, axis=1).reshape(lines_here, line_count, block_units)
    columns = jnp.pad(columns, ((0, 0), (0, 0), (0, extra_rows))).reshape(lines_here, -1)

    probes = jnp.concatenate(
        [
            load_share[:, None],
            jnp.where(jnp.arange(buses)[:, None] == ends[None, :], 1.0, 0.0),
        ],
        axis=1,
    )
    local_probe = jnp.dot(ptdf_rows, probes, preferred_element_type=jnp.float32, precision=HI)
    row_probe = line_total_pairs(jnp.dot(pick, local_probe, precision=HI))
    load_flows = local_probe[:, 0]
    at_ends = local_probe[:, 1:]
    row_at_ends = row_probe[:, 1:]

    sens_ends = []
    weights = []
    row_coeff_list = []
    for step in range(NC):
        initial = row_at_ends[step]
        row_coeffs = []
        for prior in range(step):
            value = initial[2 * prior] - initial[2 * prior + 1]
            for earlier in range(prior):
                value = value - row_coeffs[earlier] * (
                    sens_ends[earlier][2 * prior] - sens_ends[earlier][2 * prior + 1]
                )
            row_coeffs.append(value)
        current = initial
        for prior in range(step):
            current = current - row_coeffs[prior] * sens_ends[prior]
        ratio = ratios[step]
        weight = ratio / (1.0 + ratio * jnp.abs(current[2 * step] - current[2 * step + 1]))
        sens_ends.append(weight * current)
        weights.append(weight)
        row_coeff_list.append(row_coeffs)

    coeff_list = []
    for step in range(NC):
        coefficient = at_ends[:, 2 * step] - at_ends[:, 2 * step + 1]
        for prior in range(step):
            coefficient = coefficient - coeff_list[prior] * (
                sens_ends[prior][2 * step] - sens_ends[prior][2 * step + 1]
            )
        coeff_list.append(coefficient)

    gen_flows = jnp.dot(columns, everyone, preferred_element_type=jnp.float32, precision=HI)
    base = gen_flows - load_flows[:, None] * system_load[None, :]
    row_base = line_total(jnp.dot(pick, base, precision=HI))

    pieces = everyone.reshape(line_count, block_units + extra_rows, block_width)[:, block_units:]
    pieces = pieces.reshape(line_count, -1)[:, : NC * piece_width].reshape(line_count, NC, piece_width)
    pieces = jnp.take(pieces, jnp.array(piece_order([lax.axis_size(a) for a in LINE])), axis=0)
    all_rows = pieces.transpose(1, 0, 2).reshape(NC, buses)

    sens_list = []
    for step in range(NC):
        current = all_rows[step]
        for prior in range(step):
            current = current - row_coeff_list[step][prior] * sens_list[prior]
        sens_list.append(weights[step] * current)

    shift_list = []
    for step in range(NC):
        line_flow = row_base[step]
        for prior in range(step):
            line_flow = line_flow - row_coeff_list[step][prior] * shift_list[prior]
        shift_list.append(weights[step] * line_flow)
    flows = base
    for step in range(NC):
        flows = flows - coeff_list[step][:, None] * shift_list[step][None, :]
    return (flows, jnp.stack(sens_list))


def solution(mesh):
    torus = Mesh(
        mesh.devices.reshape(mesh.shape["snap"], 8, 4, 2), ("snap", "line_0", "line_1", "line_2")
    )
    in_specs = (
        P(LINE, None),
        P(SNAP_LINE, None),
        P(),
        P(SNAP_LINE),
        P(SNAP_LINE),
        P(),
        P("snap"),
        P(),
        P(),
        P(),
        P(),
        P(),
    )
    out_specs = (P(LINE, "snap"), P())
    return jax.shard_map(body, mesh=torus, in_specs=in_specs, out_specs=out_specs, check_vma=False)
```

```python
import jax
import jax.numpy as jnp
from jax import lax
from jax.sharding import Mesh
from jax.sharding import PartitionSpec as P

WMAX = 24
NC = 4
LINE = ("line_0", "line_1", "line_2")
SNAP_LINE = ("snap", "line_0", "line_1", "line_2")
HI = lax.Precision.HIGHEST
STAGES = (("line_2", 1), ("line_1", 1), ("line_1", 2), ("line_0", 1), ("line_0", 2), ("line_0", 4))


ramp_gain = 0.5


def line_total(x):
    for axis, step in STAGES:
        size = lax.axis_size(axis)
        x = x + lax.ppermute(x, axis, [(i, i ^ step) for i in range(size)])
    return x


def line_scatter(x):
    for axis, step in STAGES[1:]:
        size = lax.axis_size(axis)
        upper = (lax.axis_index(axis) // step) % 2 == 1
        half = x.shape[1] // 2
        keep = jnp.where(upper, x[:, half:], x[:, :half])
        give = jnp.where(upper, x[:, :half], x[:, half:])
        x = keep + lax.ppermute(give, axis, [(i, i ^ step) for i in range(size)])
    return x


def piece_order(sizes):
    line_0, line_1 = sizes
    owner_of = [0] * (line_0 * line_1)
    for chip in range(len(owner_of)):
        digits = {"line_0": chip // line_1, "line_1": chip % line_1}
        s = 0
        for axis, step in STAGES[1:]:
            s = s * 2 + (digits[axis] // step) % 2
        owner_of[s] = chip
    return owner_of


def body(
    ptdf_rows,
    plan,
    unit_bus,
    min_up,
    ramp_lag,
    load_share,
    system_load,
    corridor_order,
    corridor_buses,
    corridor_owner,
    corridor_row,
    corridor_ratio,
):
    unit_count, horizon = plan.shape
    lines_here, buses = ptdf_rows.shape
    snap_count = lax.axis_size("snap")
    line_count = lax.axis_size(LINE)
    here = lax.axis_index(LINE)

    rows_of = corridor_row[corridor_order]
    mine = corridor_owner[corridor_order] == here
    ends = corridor_buses[corridor_order].reshape(-1)
    ratios = corridor_ratio[corridor_order]
    pick = jnp.where(
        mine[:, None] & (rows_of[:, None] == jnp.arange(lines_here)[None, :]), 1.0, 0.0
    )

    row_piece = line_scatter(jnp.where(mine[:, None], jnp.take(ptdf_rows, rows_of, axis=0), 0.0))
    piece_width = row_piece.shape[1]
    packed = row_piece.reshape(-1)
    block_width = horizon // snap_count
    extra_rows = -(-packed.shape[0] // block_width)
    extra_rows += -(unit_count * snap_count + extra_rows) % 8
    packed = jnp.pad(packed, (0, extra_rows * block_width - packed.shape[0])).reshape(extra_rows, block_width)

    padded = jnp.pad(plan, ((0, 0), (WMAX, 0)))
    inverse = 1.0 / min_up.astype(jnp.float32)
    held_mean = jnp.zeros(plan.shape, jnp.float32)
    lagged = jnp.zeros(plan.shape, jnp.float32)
    for offset in range(WMAX):
        shifted = padded[:, WMAX - offset : WMAX - offset + horizon]
        held_mean = held_mean + shifted * jnp.where(offset < min_up, inverse, 0.0)[:, None]
        lagged = lagged + shifted * (ramp_lag == offset).astype(jnp.float32)[:, None]
    dispatch = held_mean + ramp_gain * (plan - lagged)
    unit_blocks = lax.all_to_all(dispatch, "snap", split_axis=1, concat_axis=0, tiled=True)
    block_units = unit_blocks.shape[0]
    everyone = lax.all_gather(
        jnp.concatenate([unit_blocks, packed], axis=0), LINE, axis=0, tiled=True
    )

    order_ids = unit_bus.reshape(snap_count, line_count, unit_count).transpose(1, 0, 2).reshape(-1)
    columns = jnp.take(ptdf_rows, order_ids, axis=1).reshape(lines_here, line_count, block_units)
    columns = jnp.pad(columns, ((0, 0), (0, 0), (0, extra_rows))).reshape(lines_here, -1)

    probes = jnp.concatenate(
        [
            load_share[:, None],
            jnp.where(jnp.arange(buses)[:, None] == ends[None, :], 1.0, 0.0),
        ],
        axis=1,
    )
    local_probe = jnp.dot(ptdf_rows, probes, preferred_element_type=jnp.float32, precision=HI)
    row_probe = line_total(jnp.dot(pick, local_probe, precision=HI))
    load_flows = local_probe[:, 0]
    at_ends = local_probe[:, 1:]
    row_at_ends = row_probe[:, 1:]

    sens_ends = []
    weights = []
    row_coeff_list = []
    for step in range(NC):
        initial = row_at_ends[step]
        row_coeffs = []
        for prior in range(step):
            value = initial[2 * prior] - initial[2 * prior + 1]
            for earlier in range(prior):
                value = value - row_coeffs[earlier] * (
                    sens_ends[earlier][2 * prior] - sens_ends[earlier][2 * prior + 1]
                )
            row_coeffs.append(value)
        current = initial
        for prior in range(step):
            current = current - row_coeffs[prior] * sens_ends[prior]
        ratio = ratios[step]
        weight = ratio / (1.0 + ratio * jnp.abs(current[2 * step] - current[2 * step + 1]))
        sens_ends.append(weight * current)
        weights.append(weight)
        row_coeff_list.append(row_coeffs)

    coeff_list = []
    for step in range(NC):
        coefficient = at_ends[:, 2 * step] - at_ends[:, 2 * step + 1]
        for prior in range(step):
            coefficient = coefficient - coeff_list[prior] * (
                sens_ends[prior][2 * step] - sens_ends[prior][2 * step + 1]
            )
        coeff_list.append(coefficient)

    gen_flows = jnp.dot(columns, everyone, preferred_element_type=jnp.float32, precision=HI)
    base = gen_flows - load_flows[:, None] * system_load[None, :]
    row_base = line_total(jnp.dot(pick, base, precision=HI))

    pieces = everyone.reshape(line_count, block_units + extra_rows, block_width)[:, block_units:]
    pieces = pieces.reshape(line_count, -1)[:, : NC * piece_width].reshape(-1, 2, NC, piece_width)
    pieces = pieces[:, 0] + pieces[:, 1]
    pieces = jnp.take(pieces, jnp.array(piece_order([lax.axis_size(a) for a in LINE[:2]])), axis=0)
    all_rows = pieces.transpose(1, 0, 2).reshape(NC, buses)

    sens_list = []
    for step in range(NC):
        current = all_rows[step]
        for prior in range(step):
            current = current - row_coeff_list[step][prior] * sens_list[prior]
        sens_list.append(weights[step] * current)

    shift_list = []
    for step in range(NC):
        line_flow = row_base[step]
        for prior in range(step):
            line_flow = line_flow - row_coeff_list[step][prior] * shift_list[prior]
        shift_list.append(weights[step] * line_flow)
    flows = base
    for step in range(NC):
        flows = flows - coeff_list[step][:, None] * shift_list[step][None, :]
    return (flows, jnp.stack(sens_list))


def solution(mesh):
    torus = Mesh(
        mesh.devices.reshape(mesh.shape["snap"], 8, 4, 2), ("snap", "line_0", "line_1", "line_2")
    )
    in_specs = (
        P(LINE, None),
        P(SNAP_LINE, None),
        P(),
        P(SNAP_LINE),
        P(SNAP_LINE),
        P(),
        P("snap"),
        P(),
        P(),
        P(),
        P(),
        P(),
    )
    out_specs = (P(LINE, "snap"), P())
    return jax.shard_map(body, mesh=torus, in_specs=in_specs, out_specs=out_specs, check_vma=False)
```

```python
import jax
import jax.numpy as jnp
from jax import lax
from jax.sharding import Mesh
from jax.sharding import PartitionSpec as P

WMAX = 24
NC = 4
LINE = ("line_0", "line_1", "line_2")
SNAP_LINE = ("snap", "line_0", "line_1", "line_2")
HI = lax.Precision.HIGHEST
STAGES = (("line_2", 1), ("line_1", 1), ("line_1", 2), ("line_0", 1), ("line_0", 2), ("line_0", 4))
SCATTER = STAGES[1:5]


ramp_gain = 0.5


def line_total(x):
    for axis, step in STAGES:
        size = lax.axis_size(axis)
        x = x + lax.ppermute(x, axis, [(i, i ^ step) for i in range(size)])
    return x


def line_scatter(x):
    for axis, step in SCATTER:
        size = lax.axis_size(axis)
        upper = (lax.axis_index(axis) // step) % 2 == 1
        half = x.shape[1] // 2
        keep = jnp.where(upper, x[:, half:], x[:, :half])
        give = jnp.where(upper, x[:, :half], x[:, half:])
        x = keep + lax.ppermute(give, axis, [(i, i ^ step) for i in range(size)])
    return x


def piece_order(sizes):
    near_0, line_1 = sizes
    owner_of = [0] * (near_0 * line_1)
    for group in range(len(owner_of)):
        digits = {"line_0": group // line_1, "line_1": group % line_1}
        s = 0
        for axis, step in SCATTER:
            s = s * 2 + (digits[axis] // step) % 2
        owner_of[s] = group
    return owner_of


def body(
    ptdf_rows,
    plan,
    unit_bus,
    min_up,
    ramp_lag,
    load_share,
    system_load,
    corridor_order,
    corridor_buses,
    corridor_owner,
    corridor_row,
    corridor_ratio,
):
    unit_count, horizon = plan.shape
    lines_here, buses = ptdf_rows.shape
    snap_count = lax.axis_size("snap")
    line_count = lax.axis_size(LINE)
    here = lax.axis_index(LINE)

    rows_of = corridor_row[corridor_order]
    mine = corridor_owner[corridor_order] == here
    ends = corridor_buses[corridor_order].reshape(-1)
    ratios = corridor_ratio[corridor_order]
    pick = jnp.where(
        mine[:, None] & (rows_of[:, None] == jnp.arange(lines_here)[None, :]), 1.0, 0.0
    )

    row_piece = line_scatter(jnp.where(mine[:, None], jnp.take(ptdf_rows, rows_of, axis=0), 0.0))
    piece_width = row_piece.shape[1]
    packed = row_piece.reshape(-1)
    block_width = horizon // snap_count
    extra_rows = -(-packed.shape[0] // block_width)
    extra_rows += -(unit_count * snap_count + extra_rows) % 8
    packed = jnp.pad(packed, (0, extra_rows * block_width - packed.shape[0])).reshape(extra_rows, block_width)

    padded = jnp.pad(plan, ((0, 0), (WMAX, 0)))
    inverse = 1.0 / min_up.astype(jnp.float32)
    held_mean = jnp.zeros(plan.shape, jnp.float32)
    lagged = jnp.zeros(plan.shape, jnp.float32)
    for offset in range(WMAX):
        shifted = padded[:, WMAX - offset : WMAX - offset + horizon]
        held_mean = held_mean + shifted * jnp.where(offset < min_up, inverse, 0.0)[:, None]
        lagged = lagged + shifted * (ramp_lag == offset).astype(jnp.float32)[:, None]
    dispatch = held_mean + ramp_gain * (plan - lagged)
    unit_blocks = lax.all_to_all(dispatch, "snap", split_axis=1, concat_axis=0, tiled=True)
    block_units = unit_blocks.shape[0]
    everyone = lax.all_gather(
        jnp.concatenate([unit_blocks, packed], axis=0), LINE, axis=0, tiled=True
    )

    order_ids = unit_bus.reshape(snap_count, line_count, unit_count).transpose(1, 0, 2).reshape(-1)
    columns = jnp.take(ptdf_rows, order_ids, axis=1).reshape(lines_here, line_count, block_units)
    columns = jnp.pad(columns, ((0, 0), (0, 0), (0, extra_rows))).reshape(lines_here, -1)

    probes = jnp.concatenate(
        [
            load_share[:, None],
            jnp.where(jnp.arange(buses)[:, None] == ends[None, :], 1.0, 0.0),
        ],
        axis=1,
    )
    local_probe = jnp.dot(ptdf_rows, probes, preferred_element_type=jnp.float32, precision=HI)
    row_probe = line_total(jnp.dot(pick, local_probe, precision=HI))
    load_flows = local_probe[:, 0]
    at_ends = local_probe[:, 1:]
    row_at_ends = row_probe[:, 1:]

    sens_ends = []
    weights = []
    row_coeff_list = []
    for step in range(NC):
        initial = row_at_ends[step]
        row_coeffs = []
        for prior in range(step):
            value = initial[2 * prior] - initial[2 * prior + 1]
            for earlier in range(prior):
                value = value - row_coeffs[earlier] * (
                    sens_ends[earlier][2 * prior] - sens_ends[earlier][2 * prior + 1]
                )
            row_coeffs.append(value)
        current = initial
        for prior in range(step):
            current = current - row_coeffs[prior] * sens_ends[prior]
        ratio = ratios[step]
        weight = ratio / (1.0 + ratio * jnp.abs(current[2 * step] - current[2 * step + 1]))
        sens_ends.append(weight * current)
        weights.append(weight)
        row_coeff_list.append(row_coeffs)

    coeff_list = []
    for step in range(NC):
        coefficient = at_ends[:, 2 * step] - at_ends[:, 2 * step + 1]
        for prior in range(step):
            coefficient = coefficient - coeff_list[prior] * (
                sens_ends[prior][2 * step] - sens_ends[prior][2 * step + 1]
            )
        coeff_list.append(coefficient)

    gen_flows = jnp.dot(columns, everyone, preferred_element_type=jnp.float32, precision=HI)
    base = gen_flows - load_flows[:, None] * system_load[None, :]
    row_base = line_total(jnp.dot(pick, base, precision=HI))

    pieces = everyone.reshape(line_count, block_units + extra_rows, block_width)[:, block_units:]
    line_0, line_1, line_2 = (lax.axis_size(a) for a in LINE)
    pieces = pieces.reshape(line_count, -1)[:, : NC * piece_width]
    pieces = pieces.reshape(2, line_0 // 2, line_1, line_2, NC, piece_width).sum(axis=(0, 3))
    pieces = pieces.reshape(-1, NC, piece_width)
    pieces = jnp.take(pieces, jnp.array(piece_order([line_0 // 2, line_1])), axis=0)
    all_rows = pieces.transpose(1, 0, 2).reshape(NC, buses)

    sens_list = []
    for step in range(NC):
        current = all_rows[step]
        for prior in range(step):
            current = current - row_coeff_list[step][prior] * sens_list[prior]
        sens_list.append(weights[step] * current)

    shift_list = []
    for step in range(NC):
        line_flow = row_base[step]
        for prior in range(step):
            line_flow = line_flow - row_coeff_list[step][prior] * shift_list[prior]
        shift_list.append(weights[step] * line_flow)
    flows = base
    for step in range(NC):
        flows = flows - coeff_list[step][:, None] * shift_list[step][None, :]
    return (flows, jnp.stack(sens_list))


def solution(mesh):
    torus = Mesh(
        mesh.devices.reshape(mesh.shape["snap"], 8, 4, 2), ("snap", "line_0", "line_1", "line_2")
    )
    in_specs = (
        P(LINE, None),
        P(SNAP_LINE, None),
        P(),
        P(SNAP_LINE),
        P(SNAP_LINE),
        P(),
        P("snap"),
        P(),
        P(),
        P(),
        P(),
        P(),
    )
    out_specs = (P(LINE, "snap"), P())
    return jax.shard_map(body, mesh=torus, in_specs=in_specs, out_specs=out_specs, check_vma=False)
```

```python
import jax
import jax.numpy as jnp
from jax import lax
from jax.sharding import Mesh
from jax.sharding import PartitionSpec as P

WMAX = 24
NC = 4
LINE = ("line_0", "line_1", "line_2")
SNAP_LINE = ("snap", "line_0", "line_1", "line_2")
HI = lax.Precision.HIGHEST
STAGES = (("line_2", 1), ("line_1", 1), ("line_1", 2), ("line_0", 1), ("line_0", 2), ("line_0", 4))
SCATTER = STAGES[1:4]


ramp_gain = 0.5


def line_total(x):
    for axis, step in STAGES:
        size = lax.axis_size(axis)
        x = x + lax.ppermute(x, axis, [(i, i ^ step) for i in range(size)])
    return x


def line_scatter(x):
    for axis, step in SCATTER:
        size = lax.axis_size(axis)
        upper = (lax.axis_index(axis) // step) % 2 == 1
        half = x.shape[1] // 2
        keep = jnp.where(upper, x[:, half:], x[:, :half])
        give = jnp.where(upper, x[:, :half], x[:, half:])
        x = keep + lax.ppermute(give, axis, [(i, i ^ step) for i in range(size)])
    return x


def piece_order(sizes):
    near_0, line_1 = sizes
    owner_of = [0] * (near_0 * line_1)
    for group in range(len(owner_of)):
        digits = {"line_0": group // line_1, "line_1": group % line_1}
        s = 0
        for axis, step in SCATTER:
            s = s * 2 + (digits[axis] // step) % 2
        owner_of[s] = group
    return owner_of


def body(
    ptdf_rows,
    plan,
    unit_bus,
    min_up,
    ramp_lag,
    load_share,
    system_load,
    corridor_order,
    corridor_buses,
    corridor_owner,
    corridor_row,
    corridor_ratio,
):
    unit_count, horizon = plan.shape
    lines_here, buses = ptdf_rows.shape
    snap_count = lax.axis_size("snap")
    line_count = lax.axis_size(LINE)
    here = lax.axis_index(LINE)

    rows_of = corridor_row[corridor_order]
    mine = corridor_owner[corridor_order] == here
    ends = corridor_buses[corridor_order].reshape(-1)
    ratios = corridor_ratio[corridor_order]
    pick = jnp.where(
        mine[:, None] & (rows_of[:, None] == jnp.arange(lines_here)[None, :]), 1.0, 0.0
    )

    row_piece = line_scatter(jnp.where(mine[:, None], jnp.take(ptdf_rows, rows_of, axis=0), 0.0))
    piece_width = row_piece.shape[1]
    packed = row_piece.reshape(-1)
    block_width = horizon // snap_count
    extra_rows = -(-packed.shape[0] // block_width)
    extra_rows += -(unit_count * snap_count + extra_rows) % 8
    packed = jnp.pad(packed, (0, extra_rows * block_width - packed.shape[0])).reshape(extra_rows, block_width)

    padded = jnp.pad(plan, ((0, 0), (WMAX, 0)))
    inverse = 1.0 / min_up.astype(jnp.float32)
    held_mean = jnp.zeros(plan.shape, jnp.float32)
    lagged = jnp.zeros(plan.shape, jnp.float32)
    for offset in range(WMAX):
        shifted = padded[:, WMAX - offset : WMAX - offset + horizon]
        held_mean = held_mean + shifted * jnp.where(offset < min_up, inverse, 0.0)[:, None]
        lagged = lagged + shifted * (ramp_lag == offset).astype(jnp.float32)[:, None]
    dispatch = held_mean + ramp_gain * (plan - lagged)
    unit_blocks = lax.all_to_all(dispatch, "snap", split_axis=1, concat_axis=0, tiled=True)
    block_units = unit_blocks.shape[0]
    everyone = lax.all_gather(
        jnp.concatenate([unit_blocks, packed], axis=0), LINE, axis=0, tiled=True
    )

    order_ids = unit_bus.reshape(snap_count, line_count, unit_count).transpose(1, 0, 2).reshape(-1)
    columns = jnp.take(ptdf_rows, order_ids, axis=1).reshape(lines_here, line_count, block_units)
    columns = jnp.pad(columns, ((0, 0), (0, 0), (0, extra_rows))).reshape(lines_here, -1)

    probes = jnp.concatenate(
        [
            load_share[:, None],
            jnp.where(jnp.arange(buses)[:, None] == ends[None, :], 1.0, 0.0),
        ],
        axis=1,
    )
    local_probe = jnp.dot(ptdf_rows, probes, preferred_element_type=jnp.float32, precision=HI)
    row_probe = line_total(jnp.dot(pick, local_probe, precision=HI))
    load_flows = local_probe[:, 0]
    at_ends = local_probe[:, 1:]
    row_at_ends = row_probe[:, 1:]

    sens_ends = []
    weights = []
    row_coeff_list = []
    for step in range(NC):
        initial = row_at_ends[step]
        row_coeffs = []
        for prior in range(step):
            value = initial[2 * prior] - initial[2 * prior + 1]
            for earlier in range(prior):
                value = value - row_coeffs[earlier] * (
                    sens_ends[earlier][2 * prior] - sens_ends[earlier][2 * prior + 1]
                )
            row_coeffs.append(value)
        current = initial
        for prior in range(step):
            current = current - row_coeffs[prior] * sens_ends[prior]
        ratio = ratios[step]
        weight = ratio / (1.0 + ratio * jnp.abs(current[2 * step] - current[2 * step + 1]))
        sens_ends.append(weight * current)
        weights.append(weight)
        row_coeff_list.append(row_coeffs)

    coeff_list = []
    for step in range(NC):
        coefficient = at_ends[:, 2 * step] - at_ends[:, 2 * step + 1]
        for prior in range(step):
            coefficient = coefficient - coeff_list[prior] * (
                sens_ends[prior][2 * step] - sens_ends[prior][2 * step + 1]
            )
        coeff_list.append(coefficient)

    gen_flows = jnp.dot(columns, everyone, preferred_element_type=jnp.float32, precision=HI)
    base = gen_flows - load_flows[:, None] * system_load[None, :]
    row_base = line_total(jnp.dot(pick, base, precision=HI))

    pieces = everyone.reshape(line_count, block_units + extra_rows, block_width)[:, block_units:]
    line_0, line_1, line_2 = (lax.axis_size(a) for a in LINE)
    pieces = pieces.reshape(line_count, -1)[:, : NC * piece_width]
    pieces = pieces.reshape(4, line_0 // 4, line_1, line_2, NC, piece_width).sum(axis=(0, 3))
    pieces = pieces.reshape(-1, NC, piece_width)
    pieces = jnp.take(pieces, jnp.array(piece_order([line_0 // 4, line_1])), axis=0)
    all_rows = pieces.transpose(1, 0, 2).reshape(NC, buses)

    sens_list = []
    for step in range(NC):
        current = all_rows[step]
        for prior in range(step):
            current = current - row_coeff_list[step][prior] * sens_list[prior]
        sens_list.append(weights[step] * current)

    shift_list = []
    for step in range(NC):
        line_flow = row_base[step]
        for prior in range(step):
            line_flow = line_flow - row_coeff_list[step][prior] * shift_list[prior]
        shift_list.append(weights[step] * line_flow)
    flows = base
    for step in range(NC):
        flows = flows - coeff_list[step][:, None] * shift_list[step][None, :]
    return (flows, jnp.stack(sens_list))


def solution(mesh):
    torus = Mesh(
        mesh.devices.reshape(mesh.shape["snap"], 8, 4, 2), ("snap", "line_0", "line_1", "line_2")
    )
    in_specs = (
        P(LINE, None),
        P(SNAP_LINE, None),
        P(),
        P(SNAP_LINE),
        P(SNAP_LINE),
        P(),
        P("snap"),
        P(),
        P(),
        P(),
        P(),
        P(),
    )
    out_specs = (P(LINE, "snap"), P())
    return jax.shard_map(body, mesh=torus, in_specs=in_specs, out_specs=out_specs, check_vma=False)
```
